256 devices in a mesh: lat: 32 (over x, z_hi, y), depth: 8 (over z_lo, core).
Axes of the slice: x: 4, y: 4, z: 8 (z_hi: 2, z_lo: 4; z = z_hi * 4 + z_lo), core: 2. Of those that a mesh axis runs over, the one named last changes fastest.
Arguments:
- saved_waves: float32 [2, 64, 8, 256, 256], P(None, 'lat', 'depth'), may hold values from -5 to 5
- object_slices: float32 [2, 8, 256, 8192], P(None, 'depth', None, 'lat'), may hold values from -5 to 5
- cotangent: float32 [2, 64, 256, 256], P(None, 'lat'), may hold values from -5 to 5
- transfer_phase: float32 [256, 256], replicated, may hold values from -3.140625 to 3.140625
- offsets: int32 [64], P('lat'), may hold values from 0 to 255
Outputs:
- object_grad: float32 [2, 8, 256, 8192], P(None, 'depth', None, 'lat')
- probe_grad: float32 [2, 256, 256], P(None, 'depth')
The draws below stay inside these ranges and needn't reach their ends.
All inputs are finite; a program needn't handle non-finite values.
Results may differ from the reference program's by a relative error of at most 0.0003.
Values sent between devices are 32-bit elements; how exact they have to be, the bound alone decides.
No kernel may reach another device: no remote copies, remote signals or barrier semaphores. Data moves between devices by JAX's collectives and lax.ppermute only.
A program may use at most 64 MiB of HBM per device.

```python
import jax
import jax.numpy as jnp
from jax import lax

PW = 256
P_DEV = 2
POS = 64
SLICES = 8
OW = 8192


def set_ends(entries, stream_key, low, top_value):
    longest = entries.shape.index(max(entries.shape))
    spots = []
    for shift in (0, 1):
        where = [jax.random.randint(jax.random.fold_in(stream_key, axis), (), 0, length) for axis, length in enumerate(entries.shape)]
        where[longest] = (where[longest] + shift) % entries.shape[longest]
        spots.append(tuple(where))
    return entries.at[spots[0]].set(low).at[spots[1]].set(top_value)


def level_of(key, dims, shards, smallest, high):
    level, own = 1.0, jax.random.fold_in(key, 6)
    for dim, parts in shards:
        steps = jnp.exp(jax.random.uniform(jax.random.fold_in(own, dim), (parts,), jnp.float32, smallest / len(shards), high / len(shards)))
        level = level * jnp.repeat(steps, dims[dim] // parts).reshape([-1 if axis == dim else 1 for axis in range(len(dims))])
    return level


def scatter_about(key, extent, spread, limit, pieces=(), kind=jnp.bfloat16):
    result = spread * jax.random.normal(key, extent, jnp.float32)
    if pieces:
        result = result * level_of(key, extent, pieces, -0.22, 0.18)
    return jnp.clip(result, -limit, limit).astype(kind)


def setup_inputs(seed: int = 0) -> dict:
    keys = jax.random.split(jax.random.key(seed), 6)
    return {
        "saved_waves": scatter_about(keys[0], (2, POS, SLICES, PW, PW), 0.7, 5.0, ((1, 32), (2, 8)), jnp.float32),
        "object_slices": scatter_about(keys[1], (2, SLICES, PW, OW), 0.7, 5.0, ((1, 8), (3, 32)), jnp.float32),
        "cotangent": scatter_about(keys[2], (2, POS, PW, PW), 0.7, 5.0, ((1, 32),), jnp.float32),
        "transfer_phase": jnp.clip(jax.random.uniform(keys[3], (PW, PW), jnp.float32, -3.140625, 3.140625), -3.140625, 3.140625),
        "offsets": set_ends(jax.random.randint(keys[4], (POS,), 0, PW), jax.random.fold_in(keys[4], 1), 0, PW - 1).astype(jnp.int32),
    }


def reference(saved_waves, object_slices, cotangent, transfer_phase, offsets):
    prop = jnp.exp(1j * transfer_phase)
    obj = object_slices[0] + 1j * object_slices[1]
    waves = saved_waves[0] + 1j * saved_waves[1]
    cotan = cotangent[0] + 1j * cotangent[1]
    position_ids = jnp.arange(POS, dtype=jnp.int32)
    starts = (position_ids // P_DEV) * PW + offsets.astype(jnp.int32)
    column_ids = jnp.arange(PW, dtype=jnp.int32)

    def one_position(carry, index):
        grad_acc, probe_acc = carry
        columns = (starts[index] + column_ids) % OW
        patches = jnp.take(obj, columns, axis=2)
        wave = cotan[index]
        deltas = []
        for layer in reversed(range(SLICES)):
            back = jnp.fft.ifft2(jnp.conj(prop) * jnp.fft.fft2(wave, norm="ortho"), norm="ortho")
            deltas.append(jnp.conj(waves[index, layer]) * back)
            wave = jnp.conj(patches[layer]) * back
        stacked = jnp.stack(deltas[::-1])
        grad_acc = grad_acc.at[:, :, columns].add(stacked)
        return (grad_acc, probe_acc + wave), None

    init = (jnp.zeros_like(obj), jnp.zeros_like(cotan[0]))
    (grad_acc, probe_acc), _ = lax.scan(one_position, init, position_ids)
    object_grad = jnp.stack([jnp.real(grad_acc), jnp.imag(grad_acc)])
    probe_grad = jnp.stack([jnp.real(probe_acc), jnp.imag(probe_acc)])
    return object_grad, probe_grad
```

```python
import math

import jax
import jax.numpy as jnp
from jax import lax
from jax.sharding import PartitionSpec as P


def from_behind(value, axis, steps):
    count = lax.axis_size(axis)
    pairs = [(source, (source + steps) % count) for source in range(count)]
    return lax.ppermute(value, axis, pairs)


def shifted(value, axis, steps):
    count = lax.axis_size(axis)
    first, last = (max(0, -steps), min(count, count - steps))
    return lax.ppermute(value, axis, [(source, source + steps) for source in range(first, last)])


def dft_tables(length):
    index = jnp.arange(length, dtype=jnp.int32)
    product = index[:, None] * index[None, :] % length
    angles = product.astype(jnp.float32) * (2.0 * math.pi / length)
    norm_scale = 1.0 / math.sqrt(length)
    return jnp.stack([jnp.cos(angles) * norm_scale, -jnp.sin(angles) * norm_scale])


PRECISION = lax.Precision.HIGH


def left(tables, field):
    return jnp.einsum("tjk,fkl->tfjl", tables, field, precision=PRECISION)


def right(field, tables):
    return jnp.einsum("fjk,tkl->ftjl", field, tables, precision=PRECISION)


def adjoint_propagate(tables, phase_cos, phase_sin, field):
    m = left(tables, field)
    half = jnp.stack([m[0, 0] - m[1, 1], m[0, 1] + m[1, 0]])
    n = right(half, tables)
    spec_re = n[0, 0] - n[1, 1]
    spec_im = n[0, 1] + n[1, 0]
    turned = jnp.stack([spec_re * phase_cos + spec_im * phase_sin, spec_im * phase_cos - spec_re * phase_sin])
    m = left(tables, turned)
    half = jnp.stack([m[0, 0] + m[1, 1], m[0, 1] - m[1, 0]])
    n = right(half, tables)
    return jnp.stack([n[0, 0] + n[1, 1], n[1, 0] - n[0, 1]])


def conj_times(a, v):
    return jnp.stack([a[0] * v[0] + a[1] * v[1], a[0] * v[1] - a[1] * v[0]])


def shards(saved_waves, object_slices, cotangent, transfer_phase, offsets):
    width = object_slices.shape[2]
    positions = offsets.shape[0]
    depth_size = lax.axis_size("depth")
    lat_size = lax.axis_size("lat")
    depth_index = lax.axis_index("depth")
    tables = dft_tables(width)
    phase_cos = jnp.cos(transfer_phase)
    phase_sin = jnp.sin(transfer_phase)
    neighbour = from_behind(object_slices[:, 0], "lat", -1)
    window = jnp.concatenate([object_slices[:, 0], neighbour], axis=2)

    def finish(item, back, grad_buffer):
        offset = offsets[item]
        patch = lax.dynamic_slice_in_dim(window, offset, width, 2)
        delta = conj_times(saved_waves[:, item, 0], back)
        wave = conj_times(patch, back)
        current = lax.dynamic_slice_in_dim(grad_buffer, offset, width, 2)
        grad_buffer = lax.dynamic_update_slice_in_dim(grad_buffer, current + delta, offset, 2)
        return wave, grad_buffer

    def make_run(item):
        def run(operands):
            field, grad_buffer = operands
            back = adjoint_propagate(tables, phase_cos, phase_sin, field)
            return finish(item, back, grad_buffer)

        return run

    def make_finish(item):
        def run(operands):
            back, grad_buffer = operands
            return finish(item, back, grad_buffer)

        return run

    def skip(operands):
        field, grad_buffer = operands
        return jnp.zeros_like(field), grad_buffer

    grad_buffer = jnp.zeros((2, width, 2 * width), jnp.float32)
    received = [None] * positions
    finals = [None] * positions
    for step in range(depth_size):
        active = depth_index == depth_size - 1 - step
        for item in range(positions):
            if step == 0:
                back = adjoint_propagate(tables, phase_cos, phase_sin, cotangent[:, item])
                out, grad_buffer = lax.cond(active, make_finish(item), skip, (back, grad_buffer))
            else:
                out, grad_buffer = lax.cond(active, make_run(item), skip, (received[item], grad_buffer))
            if step < depth_size - 1:
                received[item] = shifted(out, "depth", -1)
            else:
                finals[item] = out

    overflow = from_behind(grad_buffer[:, :, width:], "lat", 1)
    object_grad = (grad_buffer[:, :, :width] + overflow)[:, None]

    probe_sum = finals[0]
    for item in range(1, positions):
        probe_sum = probe_sum + finals[item]
    band = width // depth_size
    mine = probe_sum[:, :band]
    for target in range(1, depth_size):
        part = lax.ppermute(probe_sum[:, target * band:(target + 1) * band], "depth", [(0, target)])
        mine = mine + part
    bit = 1
    while bit < lat_size:
        mine = mine + lax.ppermute(mine, "lat", [(i, i ^ bit) for i in range(lat_size)])
        bit *= 2
    return (object_grad, mine)


def solution(mesh):
    placed = (
        P(None, "lat", "depth", None, None),
        P(None, "depth", None, "lat"),
        P(None, "lat", None, None),
        P(),
        P("lat"),
    )
    return jax.shard_map(
        shards,
        mesh=mesh,
        in_specs=placed,
        out_specs=(P(None, "depth", None, "lat"), P(None, "depth", None)),
        check_vma=False,
    )
```

```python
import math

import jax
import jax.numpy as jnp
from jax import lax
from jax.sharding import PartitionSpec as P


def from_behind(value, axis, steps):
    count = lax.axis_size(axis)
    pairs = [(source, (source + steps) % count) for source in range(count)]
    return lax.ppermute(value, axis, pairs)


def shifted(value, axis, steps):
    count = lax.axis_size(axis)
    first, last = (max(0, -steps), min(count, count - steps))
    return lax.ppermute(value, axis, [(source, source + steps) for source in range(first, last)])


def dft_tables(length):
    index = jnp.arange(length, dtype=jnp.int32)
    product = index[:, None] * index[None, :] % length
    angles = product.astype(jnp.float32) * (2.0 * math.pi / length)
    norm_scale = 1.0 / math.sqrt(length)
    return (jnp.cos(angles) * norm_scale, -jnp.sin(angles) * norm_scale)


def left_product(table, field):
    return jnp.einsum("jk,kl->jl", table, field, precision=lax.Precision.HIGHEST)


def right_product(table, field):
    return jnp.einsum("jk,kl->jl", field, table, precision=lax.Precision.HIGHEST)


def transform(tables, field_re, field_im, inverse):
    table_re, table_im = tables
    if inverse:
        table_im = -table_im
    half_re = left_product(table_re, field_re) - left_product(table_im, field_im)
    half_im = left_product(table_re, field_im) + left_product(table_im, field_re)
    full_re = right_product(table_re, half_re) - right_product(table_im, half_im)
    full_im = right_product(table_re, half_im) + right_product(table_im, half_re)
    return (full_re, full_im)


def adjoint_propagate(tables, phase_cos, phase_sin, field):
    spec_re, spec_im = transform(tables, field[0], field[1], False)
    turned_re = spec_re * phase_cos + spec_im * phase_sin
    turned_im = spec_im * phase_cos - spec_re * phase_sin
    return jnp.stack(transform(tables, turned_re, turned_im, True))


def conj_times(a, v):
    return jnp.stack([a[0] * v[0] + a[1] * v[1], a[0] * v[1] - a[1] * v[0]])


def shards(saved_waves, object_slices, cotangent, transfer_phase, offsets):
    width = object_slices.shape[2]
    positions = offsets.shape[0]
    depth_size = lax.axis_size("depth")
    lat_size = lax.axis_size("lat")
    depth_index = lax.axis_index("depth")
    tables = dft_tables(width)
    phase_cos = jnp.cos(transfer_phase)
    phase_sin = jnp.sin(transfer_phase)
    neighbour = from_behind(object_slices[:, 0], "lat", -1)
    window = jnp.concatenate([object_slices[:, 0], neighbour], axis=2)

    patches = [lax.dynamic_slice_in_dim(window, offsets[item], width, 2) for item in range(positions)]

    def make_run(item):
        def run(field):
            back = adjoint_propagate(tables, phase_cos, phase_sin, field)
            return conj_times(patches[item], back), back

        return run

    def make_finish(item):
        def run(back):
            return conj_times(patches[item], back), back

        return run

    def skip(field):
        return jnp.zeros_like(field), jnp.zeros_like(field)

    grad_buffer = jnp.zeros((2, width, 2 * width), jnp.float32)
    received = [None] * positions
    finals = [None] * positions
    kept = [None] * positions
    for step in range(depth_size):
        active = depth_index == depth_size - 1 - step
        for item in range(positions):
            if step == 0:
                back = adjoint_propagate(tables, phase_cos, phase_sin, cotangent[:, item])
                out, back = lax.cond(active, make_finish(item), skip, back)
                kept[item] = back
            else:
                out, back = lax.cond(active, make_run(item), skip, received[item])
                kept[item] = kept[item] + back
            if step < depth_size - 1:
                received[item] = shifted(out, "depth", -1)
            else:
                finals[item] = out
                offset = offsets[item]
                delta = conj_times(saved_waves[:, item, 0], kept[item])
                current = lax.dynamic_slice_in_dim(grad_buffer, offset, width, 2)
                grad_buffer = lax.dynamic_update_slice_in_dim(grad_buffer, current + delta, offset, 2)

    overflow = from_behind(grad_buffer[:, :, width:], "lat", 1)
    object_grad = (grad_buffer[:, :, :width] + overflow)[:, None]

    probe_sum = finals[0]
    for item in range(1, positions):
        probe_sum = probe_sum + finals[item]
    band = width // depth_size
    mine = probe_sum[:, :band]
    for target in range(1, depth_size):
        part = lax.ppermute(probe_sum[:, target * band:(target + 1) * band], "depth", [(0, target)])
        mine = mine + part
    bit = 1
    while bit < lat_size:
        mine = mine + lax.ppermute(mine, "lat", [(i, i ^ bit) for i in range(lat_size)])
        bit *= 2
    return (object_grad, mine)


def solution(mesh):
    placed = (
        P(None, "lat", "depth", None, None),
        P(None, "depth", None, "lat"),
        P(None, "lat", None, None),
        P(),
        P("lat"),
    )
    return jax.shard_map(
        shards,
        mesh=mesh,
        in_specs=placed,
        out_specs=(P(None, "depth", None, "lat"), P(None, "depth", None)),
        check_vma=False,
    )
```

```python
import math

import jax
import jax.numpy as jnp
from jax import lax
from jax.sharding import PartitionSpec as P


def from_behind(value, axis, steps):
    count = lax.axis_size(axis)
    pairs = [(source, (source + steps) % count) for source in range(count)]
    return lax.ppermute(value, axis, pairs)


def shifted(value, axis, steps):
    count = lax.axis_size(axis)
    first, last = (max(0, -steps), min(count, count - steps))
    return lax.ppermute(value, axis, [(source, source + steps) for source in range(first, last)])


def dft_tables(length):
    index = jnp.arange(length, dtype=jnp.int32)
    product = index[:, None] * index[None, :] % length
    angles = product.astype(jnp.float32) * (2.0 * math.pi / length)
    norm_scale = 1.0 / math.sqrt(length)
    return (jnp.cos(angles) * norm_scale, -jnp.sin(angles) * norm_scale)


def product(a, b):
    return jnp.einsum("jk,kl->jl", a, b, precision=lax.Precision.HIGHEST)


def gauss_tables(table_re, table_im):
    return (table_re, table_re + table_im, table_im - table_re)


def transform(tables, field_re, field_im):
    plain, summed, differed = tables
    first = product(plain, field_re + field_im)
    half_re = first - product(summed, field_im)
    half_im = first + product(differed, field_re)
    first = product(half_re + half_im, plain)
    full_re = first - product(half_im, summed)
    full_im = first + product(half_re, differed)
    return (full_re, full_im)


def adjoint_propagate(tables, phase_cos, phase_sin, field):
    forward, inverse = tables
    spec_re, spec_im = transform(forward, field[0], field[1])
    turned_re = spec_re * phase_cos + spec_im * phase_sin
    turned_im = spec_im * phase_cos - spec_re * phase_sin
    return jnp.stack(transform(inverse, turned_re, turned_im))


def conj_times(a, v):
    return jnp.stack([a[0] * v[0] + a[1] * v[1], a[0] * v[1] - a[1] * v[0]])


def shards(saved_waves, object_slices, cotangent, transfer_phase, offsets):
    width = object_slices.shape[2]
    positions = offsets.shape[0]
    depth_size = lax.axis_size("depth")
    lat_size = lax.axis_size("lat")
    depth_index = lax.axis_index("depth")
    table_re, table_im = dft_tables(width)
    tables = (gauss_tables(table_re, table_im), gauss_tables(table_re, -table_im))
    phase_cos = jnp.cos(transfer_phase)
    phase_sin = jnp.sin(transfer_phase)
    neighbour = from_behind(object_slices[:, 0], "lat", -1)
    window = jnp.concatenate([object_slices[:, 0], neighbour], axis=2)

    patches = [lax.dynamic_slice_in_dim(window, offsets[item], width, 2) for item in range(positions)]

    def make_run(item):
        def run(field):
            back = adjoint_propagate(tables, phase_cos, phase_sin, field)
            return conj_times(patches[item], back), back

        return run

    def make_finish(item):
        def run(back):
            return conj_times(patches[item], back), back

        return run

    def skip(field):
        return jnp.zeros_like(field), jnp.zeros_like(field)

    grad_buffer = jnp.zeros((2, width, 2 * width), jnp.float32)
    received = [None] * positions
    finals = [None] * positions
    kept = [None] * positions
    for step in range(depth_size):
        active = depth_index == depth_size - 1 - step
        for item in range(positions):
            if step == 0:
                back = adjoint_propagate(tables, phase_cos, phase_sin, cotangent[:, item])
                out, back = lax.cond(active, make_finish(item), skip, back)
                kept[item] = back
            else:
                out, back = lax.cond(active, make_run(item), skip, received[item])
                kept[item] = kept[item] + back
            if step < depth_size - 1:
                received[item] = shifted(out, "depth", -1)
            else:
                finals[item] = out
                offset = offsets[item]
                delta = conj_times(saved_waves[:, item, 0], kept[item])
                current = lax.dynamic_slice_in_dim(grad_buffer, offset, width, 2)
                grad_buffer = lax.dynamic_update_slice_in_dim(grad_buffer, current + delta, offset, 2)

    overflow = from_behind(grad_buffer[:, :, width:], "lat", 1)
    object_grad = (grad_buffer[:, :, :width] + overflow)[:, None]

    probe_sum = finals[0]
    for item in range(1, positions):
        probe_sum = probe_sum + finals[item]
    band = width // depth_size
    pieces = probe_sum.reshape(2, depth_size, band, width)
    pieces = lax.all_to_all(pieces, "depth", 1, 1, tiled=True)
    mine = pieces[:, 0]
    for source in range(1, depth_size):
        mine = mine + pieces[:, source]
    bit = 1
    while bit < lat_size:
        if 2 * bit < lat_size:
            low = lax.ppermute(mine, "lat", [(i, i ^ bit) for i in range(lat_size)])
            high = lax.ppermute(mine, "lat", [(i, i ^ (2 * bit)) for i in range(lat_size)])
            both = lax.ppermute(mine, "lat", [(i, i ^ (3 * bit)) for i in range(lat_size)])
            mine = (mine + low) + (high + both)
            bit *= 4
        else:
            mine = mine + lax.ppermute(mine, "lat", [(i, i ^ bit) for i in range(lat_size)])
            bit *= 2
    return (object_grad, mine)


def solution(mesh):
    placed = (
        P(None, "lat", "depth", None, None),
        P(None, "depth", None, "lat"),
        P(None, "lat", None, None),
        P(),
        P("lat"),
    )
    return jax.shard_map(
        shards,
        mesh=mesh,
        in_specs=placed,
        out_specs=(P(None, "depth", None, "lat"), P(None, "depth", None)),
        check_vma=False,
    )
```

```python
import math

import jax
import jax.numpy as jnp
from jax import lax
from jax.sharding import PartitionSpec as P


def from_behind(value, axis, steps):
    count = lax.axis_size(axis)
    pairs = [(source, (source + steps) % count) for source in range(count)]
    return lax.ppermute(value, axis, pairs)


def shifted(value, axis, steps):
    count = lax.axis_size(axis)
    first, last = (max(0, -steps), min(count, count - steps))
    return lax.ppermute(value, axis, [(source, source + steps) for source in range(first, last)])


def dft_tables(length):
    index = jnp.arange(length, dtype=jnp.int32)
    product = index[:, None] * index[None, :] % length
    angles = product.astype(jnp.float32) * (2.0 * math.pi / length)
    norm_scale = 1.0 / math.sqrt(length)
    return (jnp.cos(angles) * norm_scale, -jnp.sin(angles) * norm_scale)


def product(a, b):
    return jnp.einsum("jk,kl->jl", a, b, precision=lax.Precision.HIGHEST)


def gauss_tables(table_re, table_im):
    return (table_re, table_re + table_im, table_im - table_re)


def transform(tables, field_re, field_im):
    plain, summed, differed = tables
    first = product(plain, field_re + field_im)
    half_re = first - product(summed, field_im)
    half_im = first + product(differed, field_re)
    first = product(half_re + half_im, plain)
    full_re = first - product(half_im, summed)
    full_im = first + product(half_re, differed)
    return (full_re, full_im)


def adjoint_propagate(tables, phase_cos, phase_sin, field):
    forward, inverse = tables
    spec_re, spec_im = transform(forward, field[0], field[1])
    turned_re = spec_re * phase_cos + spec_im * phase_sin
    turned_im = spec_im * phase_cos - spec_re * phase_sin
    return jnp.stack(transform(inverse, turned_re, turned_im))


def conj_times(a, v):
    return jnp.stack([a[0] * v[0] + a[1] * v[1], a[0] * v[1] - a[1] * v[0]])


def shards(saved_waves, object_slices, cotangent, transfer_phase, offsets):
    width = object_slices.shape[2]
    positions = offsets.shape[0]
    depth_size = lax.axis_size("depth")
    lat_size = lax.axis_size("lat")
    depth_index = lax.axis_index("depth")
    table_re, table_im = dft_tables(width)
    tables = (gauss_tables(table_re, table_im), gauss_tables(table_re, -table_im))
    phase_cos = jnp.cos(transfer_phase)
    phase_sin = jnp.sin(transfer_phase)
    neighbour = from_behind(object_slices[:, 0], "lat", -1)
    window = jnp.concatenate([object_slices[:, 0], neighbour], axis=2)

    patches = [lax.dynamic_slice_in_dim(window, offsets[item], width, 2) for item in range(positions)]

    def make_run(item):
        def run(field):
            back = adjoint_propagate(tables, phase_cos, phase_sin, field)
            return conj_times(patches[item], back), back

        return run

    def make_finish(item):
        def run(back):
            return conj_times(patches[item], back), back

        return run

    def skip(field):
        return jnp.zeros_like(field), jnp.zeros_like(field)

    zeros = jnp.zeros((2, width, width), jnp.float32)

    def placed_window(kept):
        window_grad = None
        for item in range(positions):
            delta = conj_times(saved_waves[:, item, 0], kept[item])
            padded = jnp.concatenate([zeros, delta, zeros], axis=2)
            part = lax.dynamic_slice_in_dim(padded, width - offsets[item], 2 * width, 2)
            window_grad = part if window_grad is None else window_grad + part
        return window_grad

    def overflow_from(window_grad, sources):
        pairs = [
            (tile * depth_size + layer, ((tile + 1) % lat_size) * depth_size + layer)
            for tile in range(lat_size)
            for layer in sources
        ]
        return lax.ppermute(window_grad[:, :, width:], ("lat", "depth"), pairs)

    received = [None] * positions
    finals = [None] * positions
    kept = [None] * positions
    for step in range(depth_size):
        active = depth_index == depth_size - 1 - step
        for item in range(positions):
            if step == 0:
                back = adjoint_propagate(tables, phase_cos, phase_sin, cotangent[:, item])
                out, back = lax.cond(active, make_finish(item), skip, back)
                kept[item] = back
            else:
                out, back = lax.cond(active, make_run(item), skip, received[item])
                kept[item] = kept[item] + back
            if step < depth_size - 1:
                received[item] = shifted(out, "depth", -1)
            else:
                finals[item] = out
        if step == depth_size - 2:
            early = placed_window(kept)
            early_overflow = overflow_from(early, range(1, depth_size))

    late = placed_window(kept)
    late_overflow = overflow_from(late, [0])
    is_last = depth_index == 0
    main = jnp.where(is_last, late[:, :, :width], early[:, :, :width])
    object_grad = (main + (early_overflow + late_overflow))[:, None]

    probe_sum = finals[0]
    for item in range(1, positions):
        probe_sum = probe_sum + finals[item]
    band = width // depth_size
    pieces = probe_sum.reshape(2, depth_size, band, width)
    pieces = lax.all_to_all(pieces, "depth", 1, 1, tiled=True)
    mine = pieces[:, 0]
    for source in range(1, depth_size):
        mine = mine + pieces[:, source]
    bit = 1
    while bit < lat_size:
        if 2 * bit < lat_size:
            low = lax.ppermute(mine, "lat", [(i, i ^ bit) for i in range(lat_size)])
            high = lax.ppermute(mine, "lat", [(i, i ^ (2 * bit)) for i in range(lat_size)])
            both = lax.ppermute(mine, "lat", [(i, i ^ (3 * bit)) for i in range(lat_size)])
            mine = (mine + low) + (high + both)
            bit *= 4
        else:
            mine = mine + lax.ppermute(mine, "lat", [(i, i ^ bit) for i in range(lat_size)])
            bit *= 2
    return (object_grad, mine)


def solution(mesh):
    placed = (
        P(None, "lat", "depth", None, None),
        P(None, "depth", None, "lat"),
        P(None, "lat", None, None),
        P(),
        P("lat"),
    )
    return jax.shard_map(
        shards,
        mesh=mesh,
        in_specs=placed,
        out_specs=(P(None, "depth", None, "lat"), P(None, "depth", None)),
        check_vma=False,
    )
```

```python
import math

import jax
import jax.numpy as jnp
from jax import lax
from jax.sharding import PartitionSpec as P


def from_behind(value, axis, steps):
    count = lax.axis_size(axis)
    pairs = [(source, (source + steps) % count) for source in range(count)]
    return lax.ppermute(value, axis, pairs)


def shifted(value, axis, steps):
    count = lax.axis_size(axis)
    first, last = (max(0, -steps), min(count, count - steps))
    return lax.ppermute(value, axis, [(source, source + steps) for source in range(first, last)])


def dft_tables(length):
    index = jnp.arange(length, dtype=jnp.int32)
    product = index[:, None] * index[None, :] % length
    angles = product.astype(jnp.float32) * (2.0 * math.pi / length)
    norm_scale = 1.0 / math.sqrt(length)
    return (jnp.cos(angles) * norm_scale, -jnp.sin(angles) * norm_scale)


def product(a, b):
    return jnp.einsum("jk,kl->jl", a, b, precision=lax.Precision.HIGHEST)


def gauss_tables(table_re, table_im):
    return (table_re, table_re + table_im, table_im - table_re)


def transform(tables, field_re, field_im, materialize=False):
    plain, summed, differed = tables
    field_sum = field_re + field_im
    if materialize:
        field_sum, field_re, field_im = lax.optimization_barrier((field_sum, field_re * 1.0, field_im * 1.0))
    first = product(plain, field_sum)
    half_re = first - product(summed, field_im)
    half_im = first + product(differed, field_re)
    first = product(half_re + half_im, plain)
    full_re = first - product(half_im, summed)
    full_im = first + product(half_re, differed)
    return (full_re, full_im)


def adjoint_propagate(tables, phase_cos, phase_sin, field, materialize=False):
    forward, inverse = tables
    spec_re, spec_im = transform(forward, field[0], field[1], materialize)
    turned_re = spec_re * phase_cos + spec_im * phase_sin
    turned_im = spec_im * phase_cos - spec_re * phase_sin
    return jnp.stack(transform(inverse, turned_re, turned_im))


def conj_times(a, v):
    return jnp.stack([a[0] * v[0] + a[1] * v[1], a[0] * v[1] - a[1] * v[0]])


def shards(saved_waves, object_slices, cotangent, transfer_phase, offsets):
    width = object_slices.shape[2]
    positions = offsets.shape[0]
    depth_size = lax.axis_size("depth")
    lat_size = lax.axis_size("lat")
    depth_index = lax.axis_index("depth")
    table_re, table_im = dft_tables(width)
    tables = (gauss_tables(table_re, table_im), gauss_tables(table_re, -table_im))
    phase_cos = jnp.cos(transfer_phase)
    phase_sin = jnp.sin(transfer_phase)
    neighbour = from_behind(object_slices[:, 0], "lat", -1)
    window = jnp.concatenate([object_slices[:, 0], neighbour], axis=2)

    patches = [lax.dynamic_slice_in_dim(window, offsets[item], width, 2) for item in range(positions)]

    def make_run(item):
        def run(field):
            back = adjoint_propagate(tables, phase_cos, phase_sin, field, True)
            return conj_times(patches[item], back), back

        return run

    def make_finish(item):
        def run(back):
            return conj_times(patches[item], back), back

        return run

    def skip(field):
        return jnp.zeros_like(field), jnp.zeros_like(field)

    zeros = jnp.zeros((2, width, width), jnp.float32)

    def placed_window(kept):
        window_grad = None
        for item in range(positions):
            delta = conj_times(saved_waves[:, item, 0], kept[item])
            padded = jnp.concatenate([zeros, delta, zeros], axis=2)
            part = lax.dynamic_slice_in_dim(padded, width - offsets[item], 2 * width, 2)
            window_grad = part if window_grad is None else window_grad + part
        return window_grad

    def overflow_from(window_grad, sources):
        pairs = [
            (tile * depth_size + layer, ((tile + 1) % lat_size) * depth_size + layer)
            for tile in range(lat_size)
            for layer in sources
        ]
        return lax.ppermute(window_grad[:, :, width:], ("lat", "depth"), pairs)

    received = [None] * positions
    finals = [None] * positions
    kept = [None] * positions
    for step in range(depth_size):
        active = depth_index == depth_size - 1 - step
        for item in range(positions):
            if step == 0:
                back = adjoint_propagate(tables, phase_cos, phase_sin, cotangent[:, item])
                out, back = lax.cond(active, make_finish(item), skip, back)
                kept[item] = back
            else:
                field = received[item]
                if step == depth_size - 1 and item == 0:
                    early_overflow = overflow_from(early, range(1, depth_size))
                    early_overflow, field = lax.optimization_barrier((early_overflow, field))
                out, back = lax.cond(active, make_run(item), skip, field)
                kept[item] = kept[item] + back
            if step < depth_size - 1:
                received[item] = shifted(out, "depth", -1)
            else:
                finals[item] = out
        if step == depth_size - 2:
            early = placed_window(kept)

    late = placed_window(kept)
    late_overflow = overflow_from(late, [0])
    is_last = depth_index == 0
    main = jnp.where(is_last, late[:, :, :width], early[:, :, :width])
    object_grad = (main + (early_overflow + late_overflow))[:, None]

    probe_sum = finals[0]
    for item in range(1, positions):
        probe_sum = probe_sum + finals[item]
    band = width // depth_size
    pieces = probe_sum.reshape(2, depth_size, band, width)
    pieces = lax.all_to_all(pieces, "depth", 1, 1, tiled=True)
    mine = pieces[:, 0]
    for source in range(1, depth_size):
        mine = mine + pieces[:, source]
    bit = 1
    while bit < lat_size:
        if 2 * bit < lat_size:
            low = lax.ppermute(mine, "lat", [(i, i ^ bit) for i in range(lat_size)])
            high = lax.ppermute(mine, "lat", [(i, i ^ (2 * bit)) for i in range(lat_size)])
            both = lax.ppermute(mine, "lat", [(i, i ^ (3 * bit)) for i in range(lat_size)])
            mine = (mine + low) + (high + both)
            bit *= 4
        else:
            mine = mine + lax.ppermute(mine, "lat", [(i, i ^ bit) for i in range(lat_size)])
            bit *= 2
    return (object_grad, mine)


def solution(mesh):
    placed = (
        P(None, "lat", "depth", None, None),
        P(None, "depth", None, "lat"),
        P(None, "lat", None, None),
        P(),
        P("lat"),
    )
    return jax.shard_map(
        shards,
        mesh=mesh,
        in_specs=placed,
        out_specs=(P(None, "depth", None, "lat"), P(None, "depth", None)),
        check_vma=False,
    )
```

```python
import math

import jax
import jax.numpy as jnp
from jax import lax
from jax.sharding import PartitionSpec as P


def from_behind(value, axis, steps):
    count = lax.axis_size(axis)
    pairs = [(source, (source + steps) % count) for source in range(count)]
    return lax.ppermute(value, axis, pairs)


def shifted(value, axis, steps):
    count = lax.axis_size(axis)
    first, last = (max(0, -steps), min(count, count - steps))
    return lax.ppermute(value, axis, [(source, source + steps) for source in range(first, last)])


def dft_tables(length):
    index = jnp.arange(length, dtype=jnp.int32)
    product = index[:, None] * index[None, :] % length
    angles = product.astype(jnp.float32) * (2.0 * math.pi / length)
    norm_scale = 1.0 / math.sqrt(length)
    return (jnp.cos(angles) * norm_scale, -jnp.sin(angles) * norm_scale)


def product(a, b):
    return jnp.einsum("jk,kl->jl", a, b, precision=lax.Precision.HIGHEST)


def gauss_tables(table_re, table_im):
    return (table_re, table_re + table_im, table_im - table_re)


def transform(tables, field_re, field_im, materialize=False):
    plain, summed, differed = tables
    field_sum = field_re + field_im
    if materialize:
        field_sum, field_re, field_im = lax.optimization_barrier((field_sum, field_re * 1.0, field_im * 1.0))
    first = product(plain, field_sum)
    half_re = first - product(summed, field_im)
    half_im = first + product(differed, field_re)
    first = product(half_re + half_im, plain)
    full_re = first - product(half_im, summed)
    full_im = first + product(half_re, differed)
    return (full_re, full_im)


def adjoint_propagate(tables, phase_cos, phase_sin, field, materialize=False):
    forward, inverse = tables
    spec_re, spec_im = transform(forward, field[0], field[1], materialize)
    turned_re = spec_re * phase_cos + spec_im * phase_sin
    turned_im = spec_im * phase_cos - spec_re * phase_sin
    return jnp.stack(transform(inverse, turned_re, turned_im))


def conj_times(a, v):
    return jnp.stack([a[0] * v[0] + a[1] * v[1], a[0] * v[1] - a[1] * v[0]])


def shards(saved_waves, object_slices, cotangent, transfer_phase, offsets):
    width = object_slices.shape[2]
    positions = offsets.shape[0]
    depth_size = lax.axis_size("depth")
    lat_size = lax.axis_size("lat")
    depth_index = lax.axis_index("depth")
    table_re, table_im = dft_tables(width)
    tables = (gauss_tables(table_re, table_im), gauss_tables(table_re, -table_im))
    phase_cos = jnp.cos(transfer_phase)
    phase_sin = jnp.sin(transfer_phase)

    def from_right(value, layers):
        pairs = [
            (((tile + 1) % lat_size) * depth_size + layer, tile * depth_size + layer)
            for tile in range(lat_size)
            for layer in layers
        ]
        return lax.ppermute(value, ("lat", "depth"), pairs)

    first = from_right(object_slices[:, 0], [depth_size - 1])
    rest = from_right(object_slices[:, 0], range(depth_size - 1))
    first_window = jnp.concatenate([object_slices[:, 0], first], axis=2)
    window = jnp.concatenate([object_slices[:, 0], first + rest], axis=2)

    def patches_of(source):
        return [lax.dynamic_slice_in_dim(source, offsets[item], width, 2) for item in range(positions)]

    first_patches = patches_of(first_window)
    patches = patches_of(window)

    def make_run(item, own=patches):
        def run(field):
            back = adjoint_propagate(tables, phase_cos, phase_sin, field, True)
            return conj_times(own[item], back), back

        return run

    def skip(field):
        return jnp.zeros_like(field), jnp.zeros_like(field)

    zeros = jnp.zeros((2, width, width), jnp.float32)

    def placed_window(kept):
        window_grad = None
        for item in range(positions):
            delta = conj_times(saved_waves[:, item, 0], kept[item])
            padded = jnp.concatenate([zeros, delta, zeros], axis=2)
            part = lax.dynamic_slice_in_dim(padded, width - offsets[item], 2 * width, 2)
            window_grad = part if window_grad is None else window_grad + part
        return window_grad

    received = [None] * positions
    finals = [None] * positions
    kept = [None] * positions
    for step in range(depth_size):
        active = depth_index == depth_size - 1 - step
        for item in range(positions):
            if step == 0:
                out, back = lax.cond(active, make_run(item, first_patches), skip, cotangent[:, item])
                kept[item] = back
            else:
                out, back = lax.cond(active, make_run(item), skip, received[item])
                kept[item] = kept[item] + back
            if step < depth_size - 1:
                received[item] = shifted(out, "depth", -1)
            else:
                finals[item] = out

    window_grad = placed_window(kept)
    overflow = from_behind(window_grad[:, :, width:], "lat", 1)
    object_grad = (window_grad[:, :, :width] + overflow)[:, None]

    probe_sum = finals[0]
    for item in range(1, positions):
        probe_sum = probe_sum + finals[item]
    band = width // depth_size
    pieces = probe_sum.reshape(2, depth_size, band, width)
    pieces = lax.all_to_all(pieces, "depth", 1, 1, tiled=True)
    mine = pieces[:, 0]
    for source in range(1, depth_size):
        mine = mine + pieces[:, source]
    bit = 1
    while bit < lat_size:
        if 2 * bit < lat_size:
            low = lax.ppermute(mine, "lat", [(i, i ^ bit) for i in range(lat_size)])
            high = lax.ppermute(mine, "lat", [(i, i ^ (2 * bit)) for i in range(lat_size)])
            both = lax.ppermute(mine, "lat", [(i, i ^ (3 * bit)) for i in range(lat_size)])
            mine = (mine + low) + (high + both)
            bit *= 4
        else:
            mine = mine + lax.ppermute(mine, "lat", [(i, i ^ bit) for i in range(lat_size)])
            bit *= 2
    return (object_grad, mine)


def solution(mesh):
    placed = (
        P(None, "lat", "depth", None, None),
        P(None, "depth", None, "lat"),
        P(None, "lat", None, None),
        P(),
        P("lat"),
    )
    return jax.shard_map(
        shards,
        mesh=mesh,
        in_specs=placed,
        out_specs=(P(None, "depth", None, "lat"), P(None, "depth", None)),
        check_vma=False,
    )
```

```python
import math

import jax
import jax.numpy as jnp
from jax import lax
from jax.sharding import PartitionSpec as P


def from_behind(value, axis, steps):
    count = lax.axis_size(axis)
    pairs = [(source, (source + steps) % count) for source in range(count)]
    return lax.ppermute(value, axis, pairs)


def shifted(value, axis, steps):
    count = lax.axis_size(axis)
    first, last = (max(0, -steps), min(count, count - steps))
    return lax.ppermute(value, axis, [(source, source + steps) for source in range(first, last)])


def dft_tables(length):
    index = jnp.arange(length, dtype=jnp.int32)
    product = index[:, None] * index[None, :] % length
    angles = product.astype(jnp.float32) * (2.0 * math.pi / length)
    norm_scale = 1.0 / math.sqrt(length)
    return (jnp.cos(angles) * norm_scale, -jnp.sin(angles) * norm_scale)


def product(a, b):
    return jnp.einsum("jk,kl->jl", a, b, precision=lax.Precision.HIGHEST)


def gauss_tables(table_re, table_im):
    return (table_re, table_re + table_im, table_im - table_re)


def transform(tables, field_re, field_im, materialize=False):
    plain, summed, differed = tables
    field_sum = field_re + field_im
    if materialize:
        field_sum, field_re, field_im = lax.optimization_barrier((field_sum, field_re * 1.0, field_im * 1.0))
    first = product(plain, field_sum)
    half_re = first - product(summed, field_im)
    half_im = first + product(differed, field_re)
    first = product(half_re + half_im, plain)
    full_re = first - product(half_im, summed)
    full_im = first + product(half_re, differed)
    return (full_re, full_im)


def adjoint_propagate(tables, phase_cos, phase_sin, field, materialize=False):
    forward, inverse = tables
    spec_re, spec_im = transform(forward, field[0], field[1], materialize)
    turned_re = spec_re * phase_cos + spec_im * phase_sin
    turned_im = spec_im * phase_cos - spec_re * phase_sin
    return jnp.stack(transform(inverse, turned_re, turned_im))


def conj_times(a, v):
    return jnp.stack([a[0] * v[0] + a[1] * v[1], a[0] * v[1] - a[1] * v[0]])


def shards(saved_waves, object_slices, cotangent, transfer_phase, offsets):
    width = object_slices.shape[2]
    positions = offsets.shape[0]
    depth_size = lax.axis_size("depth")
    lat_size = lax.axis_size("lat")
    depth_index = lax.axis_index("depth")
    table_re, table_im = dft_tables(width)
    tables = (gauss_tables(table_re, table_im), gauss_tables(table_re, -table_im))
    phase_cos = jnp.cos(transfer_phase)
    phase_sin = jnp.sin(transfer_phase)

    def from_right(value, layers):
        pairs = [
            (((tile + 1) % lat_size) * depth_size + layer, tile * depth_size + layer)
            for tile in range(lat_size)
            for layer in layers
        ]
        return lax.ppermute(value, ("lat", "depth"), pairs)

    first = from_right(object_slices[:, 0], [depth_size - 1])
    rest = from_right(object_slices[:, 0], range(depth_size - 1))
    first_window = jnp.concatenate([object_slices[:, 0], first], axis=2)
    window = jnp.concatenate([object_slices[:, 0], first + rest], axis=2)

    def patches_of(source):
        return [lax.dynamic_slice_in_dim(source, offsets[item], width, 2) for item in range(positions)]

    first_patches = patches_of(first_window)
    patches = patches_of(window)

    def make_run(item, own=patches):
        def run(field):
            back = adjoint_propagate(tables, phase_cos, phase_sin, field, True)
            return conj_times(own[item], back), back

        return run

    def skip(field):
        return jnp.zeros_like(field), jnp.zeros_like(field)

    zeros = jnp.zeros((2, width, width), jnp.float32)

    def placed(kept, main):
        window_part = None
        for item in range(positions):
            delta = conj_times(saved_waves[:, item, 0], kept[item])
            padded = jnp.concatenate([zeros, delta] if main else [delta, zeros], axis=2)
            part = lax.dynamic_slice_in_dim(padded, width - offsets[item], width, 2)
            window_part = part if window_part is None else window_part + part
        return window_part

    def overflow_of(kept, layer):
        pairs = [
            (tile * depth_size + layer, ((tile + 1) % lat_size) * depth_size + layer)
            for tile in range(lat_size)
        ]
        return lax.ppermute(placed(kept, False), ("lat", "depth"), pairs)

    received = [None] * positions
    finals = [None] * positions
    kept = [None] * positions
    overflows = []
    previous = None
    for step in range(depth_size):
        active = depth_index == depth_size - 1 - step
        for item in range(positions):
            field = cotangent[:, item] if step == 0 else received[item]
            if previous is not None:
                field, previous = lax.optimization_barrier((field, previous))
            if item == 0 and 2 <= step and step - 2 < depth_size - 2:
                overflows[step - 2], field = lax.optimization_barrier((overflows[step - 2], field))
            if step == 0:
                out, back = lax.cond(active, make_run(item, first_patches), skip, field)
                kept[item] = back
            else:
                out, back = lax.cond(active, make_run(item), skip, field)
                kept[item] = kept[item] + back
            previous = out
            if step < depth_size - 1:
                received[item] = shifted(out, "depth", -1)
            else:
                finals[item] = out
        if step < depth_size - 1:
            overflows.append(overflow_of(kept, depth_size - 1 - step))

    main = placed(kept, True)
    overflows.append(overflow_of(kept, 0))
    incoming = overflows[0]
    for part in overflows[1:]:
        incoming = incoming + part
    object_grad = (main + incoming)[:, None]

    probe_sum = finals[0]
    for item in range(1, positions):
        probe_sum = probe_sum + finals[item]
    band = width // depth_size
    pieces = probe_sum.reshape(2, depth_size, band, width)
    pieces = lax.all_to_all(pieces, "depth", 1, 1, tiled=True)
    mine = pieces[:, 0]
    for source in range(1, depth_size):
        mine = mine + pieces[:, source]
    bit = 1
    while bit < lat_size:
        if 2 * bit < lat_size:
            low = lax.ppermute(mine, "lat", [(i, i ^ bit) for i in range(lat_size)])
            high = lax.ppermute(mine, "lat", [(i, i ^ (2 * bit)) for i in range(lat_size)])
            both = lax.ppermute(mine, "lat", [(i, i ^ (3 * bit)) for i in range(lat_size)])
            mine = (mine + low) + (high + both)
            bit *= 4
        else:
            mine = mine + lax.ppermute(mine, "lat", [(i, i ^ bit) for i in range(lat_size)])
            bit *= 2
    return (object_grad, mine)


def solution(mesh):
    placed = (
        P(None, "lat", "depth", None, None),
        P(None, "depth", None, "lat"),
        P(None, "lat", None, None),
        P(),
        P("lat"),
    )
    return jax.shard_map(
        shards,
        mesh=mesh,
        in_specs=placed,
        out_specs=(P(None, "depth", None, "lat"), P(None, "depth", None)),
        check_vma=False,
    )
```

```python
import math

import jax
import jax.numpy as jnp
from jax import lax
from jax.sharding import PartitionSpec as P


def from_behind(value, axis, steps):
    count = lax.axis_size(axis)
    pairs = [(source, (source + steps) % count) for source in range(count)]
    return lax.ppermute(value, axis, pairs)


def shifted(value, axis, steps):
    count = lax.axis_size(axis)
    first, last = (max(0, -steps), min(count, count - steps))
    return lax.ppermute(value, axis, [(source, source + steps) for source in range(first, last)])


def dft_tables(length):
    index = jnp.arange(length, dtype=jnp.int32)
    product = index[:, None] * index[None, :] % length
    angles = product.astype(jnp.float32) * (2.0 * math.pi / length)
    norm_scale = 1.0 / math.sqrt(length)
    return (jnp.cos(angles) * norm_scale, -jnp.sin(angles) * norm_scale)


def product(a, b):
    return jnp.einsum("jk,kl->jl", a, b, precision=lax.Precision.HIGHEST)


def gauss_tables(table_re, table_im):
    return (table_re, table_re + table_im, table_im - table_re)


def transform(tables, field_re, field_im, materialize=False):
    plain, summed, differed = tables
    field_sum = field_re + field_im
    if materialize:
        field_sum, field_re, field_im = lax.optimization_barrier((field_sum, field_re * 1.0, field_im * 1.0))
    first = product(plain, field_sum)
    half_re = first - product(summed, field_im)
    half_im = first + product(differed, field_re)
    first = product(half_re + half_im, plain)
    full_re = first - product(half_im, summed)
    full_im = first + product(half_re, differed)
    return (full_re, full_im)


def adjoint_propagate(tables, phase_cos, phase_sin, field, materialize=False):
    forward, inverse = tables
    spec_re, spec_im = transform(forward, field[0], field[1], materialize)
    turned_re = spec_re * phase_cos + spec_im * phase_sin
    turned_im = spec_im * phase_cos - spec_re * phase_sin
    return jnp.stack(transform(inverse, turned_re, turned_im))


def conj_times(a, v):
    return jnp.stack([a[0] * v[0] + a[1] * v[1], a[0] * v[1] - a[1] * v[0]])


def shards(saved_waves, object_slices, cotangent, transfer_phase, offsets):
    width = object_slices.shape[2]
    positions = offsets.shape[0]
    depth_size = lax.axis_size("depth")
    lat_size = lax.axis_size("lat")
    depth_index = lax.axis_index("depth")
    table_re, table_im = dft_tables(width)
    tables = (gauss_tables(table_re, table_im), gauss_tables(table_re, -table_im))
    phase_cos = jnp.cos(transfer_phase)
    phase_sin = jnp.sin(transfer_phase)

    def from_right(value, layers):
        pairs = [
            (((tile + 1) % lat_size) * depth_size + layer, tile * depth_size + layer)
            for tile in range(lat_size)
            for layer in layers
        ]
        return lax.ppermute(value, ("lat", "depth"), pairs)

    first = from_right(object_slices[:, 0], [depth_size - 1])
    first_window = jnp.concatenate([object_slices[:, 0], first], axis=2)

    def patches_of(source):
        return [lax.dynamic_slice_in_dim(source, offsets[item], width, 2) for item in range(positions)]

    first_patches = patches_of(first_window)
    patches = None

    def make_run(item, own):
        def run(field):
            back = adjoint_propagate(tables, phase_cos, phase_sin, field, True)
            return conj_times(own[item], back), back

        return run

    def skip(field):
        return jnp.zeros_like(field), jnp.zeros_like(field)

    zeros = jnp.zeros((2, width, width), jnp.float32)

    def placed_window(kept):
        window_grad = None
        for item in range(positions):
            delta = conj_times(saved_waves[:, item, 0], kept[item])
            padded = jnp.concatenate([zeros, delta, zeros], axis=2)
            part = lax.dynamic_slice_in_dim(padded, width - offsets[item], 2 * width, 2)
            window_grad = part if window_grad is None else window_grad + part
        return window_grad

    received = [None] * positions
    finals = [None] * positions
    kept = [None] * positions
    for step in range(depth_size):
        active = depth_index == depth_size - 1 - step
        for item in range(positions):
            if step == 0:
                out, back = lax.cond(active, make_run(item, first_patches), skip, cotangent[:, item])
                kept[item] = back
                if item == 0:
                    source, out = lax.optimization_barrier((object_slices[:, 0], out))
                    rest = from_right(source, range(depth_size - 1))
                    window = jnp.concatenate([object_slices[:, 0], first + rest], axis=2)
                    patches = patches_of(window)
            else:
                out, back = lax.cond(active, make_run(item, patches), skip, received[item])
                kept[item] = kept[item] + back
            if step < depth_size - 1:
                received[item] = shifted(out, "depth", -1)
            else:
                finals[item] = out

    window_grad = placed_window(kept)
    probe_sum = finals[0]
    for item in range(1, positions):
        probe_sum = probe_sum + finals[item]
    probe_sum, window_grad = lax.optimization_barrier((probe_sum, window_grad))
    overflow = from_behind(window_grad[:, :, width:], "lat", 1)
    object_grad = (window_grad[:, :, :width] + overflow)[:, None]

    band = width // depth_size
    pieces = probe_sum.reshape(2, depth_size, band, width)
    pieces = lax.all_to_all(pieces, "depth", 1, 1, tiled=True)
    mine = pieces[:, 0]
    for source in range(1, depth_size):
        mine = mine + pieces[:, source]
    bit = 1
    while bit < lat_size:
        if 2 * bit < lat_size:
            low = lax.ppermute(mine, "lat", [(i, i ^ bit) for i in range(lat_size)])
            high = lax.ppermute(mine, "lat", [(i, i ^ (2 * bit)) for i in range(lat_size)])
            both = lax.ppermute(mine, "lat", [(i, i ^ (3 * bit)) for i in range(lat_size)])
            mine = (mine + low) + (high + both)
            bit *= 4
        else:
            mine = mine + lax.ppermute(mine, "lat", [(i, i ^ bit) for i in range(lat_size)])
            bit *= 2
    return (object_grad, mine)


def solution(mesh):
    placed = (
        P(None, "lat", "depth", None, None),
        P(None, "depth", None, "lat"),
        P(None, "lat", None, None),
        P(),
        P("lat"),
    )
    return jax.shard_map(
        shards,
        mesh=mesh,
        in_specs=placed,
        out_specs=(P(None, "depth", None, "lat"), P(None, "depth", None)),
        check_vma=False,
    )
```

```python
import math

import jax
import jax.numpy as jnp
from jax import lax
from jax.sharding import PartitionSpec as P


def from_behind(value, axis, steps):
    count = lax.axis_size(axis)
    pairs = [(source, (source + steps) % count) for source in range(count)]
    return lax.ppermute(value, axis, pairs)


def shifted(value, axis, steps):
    count = lax.axis_size(axis)
    first, last = (max(0, -steps), min(count, count - steps))
    return lax.ppermute(value, axis, [(source, source + steps) for source in range(first, last)])


def dft_tables(length):
    index = jnp.arange(length, dtype=jnp.int32)
    product = index[:, None] * index[None, :] % length
    angles = product.astype(jnp.float32) * (2.0 * math.pi / length)
    norm_scale = 1.0 / math.sqrt(length)
    return (jnp.cos(angles) * norm_scale, -jnp.sin(angles) * norm_scale)


def product(a, b):
    return jnp.einsum("jk,kl->jl", a, b, precision=lax.Precision.HIGHEST)


def gauss_tables(table_re, table_im):
    return (table_re, table_re + table_im, table_im - table_re)


def transform(tables, field_re, field_im, materialize=False):
    plain, summed, differed = tables
    field_sum = field_re + field_im
    if materialize:
        field_sum, field_re, field_im = lax.optimization_barrier((field_sum, field_re * 1.0, field_im * 1.0))
    first = product(plain, field_sum)
    half_re = first - product(summed, field_im)
    half_im = first + product(differed, field_re)
    first = product(half_re + half_im, plain)
    full_re = first - product(half_im, summed)
    full_im = first + product(half_re, differed)
    return (full_re, full_im)


def adjoint_propagate(tables, phase_cos, phase_sin, field, materialize=False):
    forward, inverse = tables
    spec_re, spec_im = transform(forward, field[0], field[1], materialize)
    turned_re = spec_re * phase_cos + spec_im * phase_sin
    turned_im = spec_im * phase_cos - spec_re * phase_sin
    return jnp.stack(transform(inverse, turned_re, turned_im))


def conj_times(a, v):
    return jnp.stack([a[0] * v[0] + a[1] * v[1], a[0] * v[1] - a[1] * v[0]])


def shards(saved_waves, object_slices, cotangent, transfer_phase, offsets):
    width = object_slices.shape[2]
    positions = offsets.shape[0]
    depth_size = lax.axis_size("depth")
    lat_size = lax.axis_size("lat")
    depth_index = lax.axis_index("depth")
    table_re, table_im = dft_tables(width)
    tables = (gauss_tables(table_re, table_im), gauss_tables(table_re, -table_im))
    phase_cos = jnp.cos(transfer_phase)
    phase_sin = jnp.sin(transfer_phase)

    def from_right(value, layers):
        pairs = [
            (((tile + 1) % lat_size) * depth_size + layer, tile * depth_size + layer)
            for tile in range(lat_size)
            for layer in layers
        ]
        return lax.ppermute(value, ("lat", "depth"), pairs)

    first = from_right(object_slices[:, 0], [depth_size - 1])
    rest = from_right(object_slices[:, 0], range(depth_size - 1))
    first_window = jnp.concatenate([object_slices[:, 0], first], axis=2)
    window = jnp.concatenate([object_slices[:, 0], first + rest], axis=2)

    def patches_of(source):
        return [lax.dynamic_slice_in_dim(source, offsets[item], width, 2) for item in range(positions)]

    first_patches = patches_of(first_window)
    patches = patches_of(window)

    def make_run(item, own=patches):
        def run(field):
            back = adjoint_propagate(tables, phase_cos, phase_sin, field, True)
            return conj_times(own[item], back), back

        return run

    def skip(field):
        return jnp.zeros_like(field), jnp.zeros_like(field)

    zeros = jnp.zeros((2, width, width), jnp.float32)

    def placed_window(kept):
        window_grad = None
        for item in range(positions):
            delta = conj_times(saved_waves[:, item, 0], kept[item])
            padded = jnp.concatenate([zeros, delta, zeros], axis=2)
            part = lax.dynamic_slice_in_dim(padded, width - offsets[item], 2 * width, 2)
            window_grad = part if window_grad is None else window_grad + part
        return window_grad

    received = [None] * positions
    finals = [None] * positions
    kept = [None] * positions
    for step in range(depth_size):
        active = depth_index == depth_size - 1 - step
        for item in range(positions):
            if step == 0:
                out, back = lax.cond(active, make_run(item, first_patches), skip, cotangent[:, item])
                kept[item] = back
            else:
                out, back = lax.cond(active, make_run(item), skip, received[item])
                kept[item] = kept[item] + back
            if step < depth_size - 1:
                received[item] = shifted(out, "depth", -1)
            else:
                finals[item] = out

    window_grad = placed_window(kept)
    overflow = from_behind(window_grad[:, :, width:], "lat", 1)
    object_grad = (window_grad[:, :, :width] + overflow)[:, None]

    probe_sum = finals[0]
    for item in range(1, positions):
        probe_sum = probe_sum + finals[item]
    band = width // depth_size
    pieces = probe_sum.reshape(2, depth_size, band, width)
    pieces = lax.all_to_all(pieces, "depth", 1, 1, tiled=True)
    mine = pieces[:, 0]
    for source in range(1, depth_size):
        mine = mine + pieces[:, source]
    rounds = [(1, 2), (8, 16), (4,)] if lat_size == 32 else [(1 << k,) for k in range(lat_size.bit_length() - 1)]
    for group in rounds:
        if len(group) == 2:
            low_bit, high_bit = group
            low = lax.ppermute(mine, "lat", [(i, i ^ low_bit) for i in range(lat_size)])
            high = lax.ppermute(mine, "lat", [(i, i ^ high_bit) for i in range(lat_size)])
            both = lax.ppermute(mine, "lat", [(i, i ^ (low_bit | high_bit)) for i in range(lat_size)])
            mine = (mine + low) + (high + both)
        else:
            mine = mine + lax.ppermute(mine, "lat", [(i, i ^ group[0]) for i in range(lat_size)])
    return (object_grad, mine)


def solution(mesh):
    placed = (
        P(None, "lat", "depth", None, None),
        P(None, "depth", None, "lat"),
        P(None, "lat", None, None),
        P(),
        P("lat"),
    )
    return jax.shard_map(
        shards,
        mesh=mesh,
        in_specs=placed,
        out_specs=(P(None, "depth", None, "lat"), P(None, "depth", None)),
        check_vma=False,
    )
```

```python
import math

import jax
import jax.numpy as jnp
from jax import lax
from jax.sharding import PartitionSpec as P


def from_behind(value, axis, steps):
    count = lax.axis_size(axis)
    pairs = [(source, (source + steps) % count) for source in range(count)]
    return lax.ppermute(value, axis, pairs)


def shifted(value, axis, steps):
    count = lax.axis_size(axis)
    first, last = (max(0, -steps), min(count, count - steps))
    return lax.ppermute(value, axis, [(source, source + steps) for source in range(first, last)])


def dft_tables(length):
    index = jnp.arange(length, dtype=jnp.int32)
    product = index[:, None] * index[None, :] % length
    angles = product.astype(jnp.float32) * (2.0 * math.pi / length)
    norm_scale = 1.0 / math.sqrt(length)
    return (jnp.cos(angles) * norm_scale, -jnp.sin(angles) * norm_scale)


def product(a, b):
    return jnp.einsum("jk,kl->jl", a, b, precision=lax.Precision.HIGHEST)


def gauss_tables(table_re, table_im):
    return (table_re, table_re + table_im, table_im - table_re)


def transform(tables, field_re, field_im, materialize=False):
    plain, summed, differed = tables
    field_sum = field_re + field_im
    if materialize:
        field_sum, field_re, field_im = lax.optimization_barrier((field_sum, field_re * 1.0, field_im * 1.0))
    first = product(plain, field_sum)
    half_re = first - product(summed, field_im)
    half_im = first + product(differed, field_re)
    first = product(half_re + half_im, plain)
    full_re = first - product(half_im, summed)
    full_im = first + product(half_re, differed)
    return (full_re, full_im)


def adjoint_propagate(tables, phase_cos, phase_sin, field, materialize=False):
    forward, inverse = tables
    spec_re, spec_im = transform(forward, field[0], field[1], materialize)
    turned_re = spec_re * phase_cos + spec_im * phase_sin
    turned_im = spec_im * phase_cos - spec_re * phase_sin
    return jnp.stack(transform(inverse, turned_re, turned_im))


def conj_times(a, v):
    return jnp.stack([a[0] * v[0] + a[1] * v[1], a[0] * v[1] - a[1] * v[0]])


def shards(saved_waves, object_slices, cotangent, transfer_phase, offsets):
    width = object_slices.shape[2]
    positions = offsets.shape[0]
    depth_size = lax.axis_size("depth")
    lat_size = lax.axis_size("lat")
    depth_index = lax.axis_index("depth")
    table_re, table_im = dft_tables(width)
    tables = (gauss_tables(table_re, table_im), gauss_tables(table_re, -table_im))
    phase_cos = jnp.cos(transfer_phase)
    phase_sin = jnp.sin(transfer_phase)

    def from_right(value, layers):
        pairs = [
            (((tile + 1) % lat_size) * depth_size + layer, tile * depth_size + layer)
            for tile in range(lat_size)
            for layer in layers
        ]
        return lax.ppermute(value, ("lat", "depth"), pairs)

    first = from_right(object_slices[:, 0], [depth_size - 1])
    rest = from_right(object_slices[:, 0], range(depth_size - 1))
    first_window = jnp.concatenate([object_slices[:, 0], first], axis=2)
    window = jnp.concatenate([object_slices[:, 0], first + rest], axis=2)

    def patches_of(source):
        return [lax.dynamic_slice_in_dim(source, offsets[item], width, 2) for item in range(positions)]

    first_patches = patches_of(first_window)
    patches = patches_of(window)

    def make_run(item, own=patches):
        def run(field):
            back = adjoint_propagate(tables, phase_cos, phase_sin, field, True)
            return conj_times(own[item], back), back

        return run

    def skip(field):
        return jnp.zeros_like(field), jnp.zeros_like(field)

    zeros = jnp.zeros((2, width, width), jnp.float32)

    def placed_window(kept):
        window_grad = None
        for item in range(positions):
            delta = conj_times(saved_waves[:, item, 0], kept[item])
            padded = jnp.concatenate([zeros, delta, zeros], axis=2)
            part = lax.dynamic_slice_in_dim(padded, width - offsets[item], 2 * width, 2)
            window_grad = part if window_grad is None else window_grad + part
        return window_grad

    received = [None] * positions
    finals = [None] * positions
    kept = [None] * positions
    for step in range(depth_size):
        active = depth_index == depth_size - 1 - step
        for item in range(positions):
            if step == 0:
                out, back = lax.cond(active, make_run(item, first_patches), skip, cotangent[:, item])
                kept[item] = back
            else:
                out, back = lax.cond(active, make_run(item), skip, received[item])
                kept[item] = kept[item] + back
            if step < depth_size - 1:
                received[item] = shifted(out, "depth", -1)
            else:
                finals[item] = out

    window_grad = placed_window(kept)
    overflow = from_behind(window_grad[:, :, width:], "lat", 1)
    object_grad = (window_grad[:, :, :width] + overflow)[:, None]

    probe_sum = finals[0]
    for item in range(1, positions):
        probe_sum = probe_sum + finals[item]
    band = width // depth_size
    pieces = probe_sum.reshape(2, depth_size, band, width)
    pieces = lax.all_to_all(pieces, "depth", 1, 1, tiled=True)
    mine = pieces[:, 0]
    for source in range(1, depth_size):
        mine = mine + pieces[:, source]
    rounds = [(8, 16), (1, 2), (4,)] if lat_size == 32 else [(1 << k,) for k in range(lat_size.bit_length() - 1)]
    for group in rounds:
        if len(group) == 2:
            low_bit, high_bit = group
            low = lax.ppermute(mine, "lat", [(i, i ^ low_bit) for i in range(lat_size)])
            high = lax.ppermute(mine, "lat", [(i, i ^ high_bit) for i in range(lat_size)])
            both = lax.ppermute(mine, "lat", [(i, i ^ (low_bit | high_bit)) for i in range(lat_size)])
            mine = (mine + low) + (high + both)
        else:
            mine = mine + lax.ppermute(mine, "lat", [(i, i ^ group[0]) for i in range(lat_size)])
    return (object_grad, mine)


def solution(mesh):
    placed = (
        P(None, "lat", "depth", None, None),
        P(None, "depth", None, "lat"),
        P(None, "lat", None, None),
        P(),
        P("lat"),
    )
    return jax.shard_map(
        shards,
        mesh=mesh,
        in_specs=placed,
        out_specs=(P(None, "depth", None, "lat"), P(None, "depth", None)),
        check_vma=False,
    )
```
